128 devices in a mesh: pipe: 4 (over z_hi, core), expert: 32 (over x, z_lo, y).
Axes of the slice: x: 4, y: 4, z: 4 (z_hi: 2, z_lo: 2; z = z_hi * 2 + z_lo), core: 2. Of those that a mesh axis runs over, the one named last changes fastest.
Arguments:
- grad_out: bfloat16 [4, 2, 2048, 2048], P('pipe', None, 'expert'), may hold values from -6 to 6
- route_weights: float32 [4, 2, 2048, 8], P('pipe', None, 'expert'), may hold values from 0.1 to 0.6
- expert_ids: int32 [4, 2, 2048, 8], P('pipe', None, 'expert'), may hold values from 0 to 31, all different within a row; in each aligned block of 64 rows (0 to 63, 64 to 127, ..., all dimensions but the last counted through in order) at most 20 rows name the same one
- hot_pos: int32 [4, 8], P('pipe'), may hold values from 0 to 3, as said below
- up_weight: bfloat16 [4, 32, 2048, 768], P('pipe', 'expert'), may hold values from -0.125 to 0.125
- down_weight: bfloat16 [4, 32, 768, 2048], P('pipe', 'expert'), may hold values from -0.21875 to 0.21875
- saved_inputs: bfloat16 [4, 2, 32, 32, 25, 2048], P('pipe', None, 'expert'), may hold values from -6 to 6
- saved_gates: bfloat16 [4, 2, 32, 32, 25, 768], P('pipe', None, 'expert'), may hold values from -8 to 8
Outputs:
- sent_back: bfloat16 [4, 2, 2048, 2048], P('pipe', None, 'expert')
- up_grad: bfloat16 [4, 32, 2048, 768], P('pipe', 'expert')
- down_grad: bfloat16 [4, 32, 768, 2048], P('pipe', 'expert')
- gate_grads: bfloat16 [4, 2, 32, 32, 25, 768], P('pipe', None, 'expert')
- hot_up_grad: bfloat16 [4, 32, 512, 768], P('pipe', 'expert')
- hot_down_grad: bfloat16 [4, 32, 192, 2048], P('pipe', 'expert')
The draws below stay inside these ranges and needn't reach their ends.
Inputs may be any that keep to these rules, and one draw needn't show every extreme that they name: `expert_ids`: each token names 8 different experts. Among the rows of one device in one micro-batch of one section no expert is named more than 20 times, a bound that some block reaches. `hot_pos`: in section 0 the first and the last group copy their expert 4 - 2; in section 1 the first group copies its expert 4 - 1 and the last group its expert 4 - 3.
All inputs are finite; a program needn't handle non-finite values.
Results may differ from the reference program's by a relative error of at most 0.0065.
Values may be sent and summed in bfloat16 or wider, within the bound.
No kernel may reach another device: no remote copies, remote signals or barrier semaphores. Data moves between devices by JAX's collectives and lax.ppermute only.
A program may use at most 192 MiB of HBM per device.

```python
import math
import jax
import jax.numpy as jnp
import numpy as np
from jax import lax

D = 2048
FF = 768
TOP = 8
REPL = 4
MB = 2
TOK_DEV = 64
SECTIONS = 4
EXPERTS = 32
HOT = 8
TOKENS = 2048
MOST = 20
SLOTS = 25


def draw_hot_pos(key, part):
    first_key = jax.random.fold_in(key, 101)
    spread = jax.random.randint(first_key, (SECTIONS, HOT), 0, REPL, dtype=jnp.int32)
    section_ix = jnp.arange(SECTIONS, dtype=jnp.int32)[:, None] + jnp.zeros((SECTIONS, HOT), jnp.int32)
    group_ix = jnp.arange(HOT, dtype=jnp.int32)[None, :] + jnp.zeros((SECTIONS, HOT), jnp.int32)
    edge_first = group_ix == 0
    edge_last = group_ix == HOT - 1
    result = jnp.where((section_ix == 0) & (edge_first | edge_last), REPL - 2, spread)
    result = jnp.where((section_ix == 1) & edge_first, REPL - 1, result)
    result = jnp.where((section_ix == 1) & edge_last, REPL - 3, result)
    return result.astype(jnp.int32)


def block_scale(own_key, shape, cuts, smallest, high):
    level, own = 1.0, jax.random.fold_in(own_key, 6)
    for axis_at, blocks in cuts:
        draws = jnp.exp(jax.random.uniform(jax.random.fold_in(own, axis_at), (blocks,), jnp.float32, smallest / len(cuts), high / len(cuts)))
        level = level * jnp.repeat(draws, shape[axis_at] // blocks).reshape([-1 if axis == axis_at else 1 for axis in range(len(shape))])
    return level


def assign_block(stream_key, own, number, rows, count, top, limit, skew):
    ranking = jax.random.permutation(stream_key, count)
    heavy_load, ordinary = portions_of(count, rows * top, limit, skew, True), portions_of(count, rows * top, limit, skew, False)
    places = jnp.arange(count)

    def named(sizes, turn):
        used = int((sizes > 0).sum())
        fixed = max(1, used // 4)
        moved = fixed + (places - fixed + turn * (used - fixed)) % max(1, count - fixed)
        return jnp.zeros((count,), jnp.int32).at[ranking[jnp.where(places < fixed, places, moved)]].set(jnp.asarray(sizes, jnp.int32))

    sizes = jnp.where(number % 4 == 0, named(heavy_load, number // 4), named(ordinary, number - number // 4 - 1))
    mixed = jax.random.permutation(jax.random.fold_in(own, 3), count)
    giver, receiver = mixed[0:count // 2 * 2:2], mixed[1:count // 2 * 2:2]
    slack = jnp.minimum(sizes[giver] - 1, limit - sizes[receiver]) // 2
    slack = jnp.where((giver == ranking[0]) | (receiver == ranking[0]) | (sizes[receiver] == 0), 0, jnp.maximum(slack, 0))
    moved = jax.random.randint(jax.random.fold_in(own, 4), (count // 2,), 0, 1 << 20) % (slack + 1)
    sizes = sizes.at[giver].add(-moved).at[receiver].add(moved)
    items = jnp.searchsorted(jnp.cumsum(sizes), jnp.arange(rows * top), side="right").astype(jnp.int32)
    table = items.reshape(top, rows).T
    table = table[jax.random.permutation(jax.random.fold_in(own, 1), rows)]
    turn = jax.random.randint(jax.random.fold_in(own, 2), (rows, 1), 0, top)
    return jnp.take_along_axis(table, (jnp.arange(top)[None, :] + turn) % top, axis=1)


def portions_of(amount, total, most, lean, full):
    weights = [(1 << 20) // math.isqrt(rank ** lean) + 1 for rank in range(1, amount + 1)]
    largest = most if full else min(most, max(-(-total // amount), total * weights[0] // sum(weights)))
    least = 1 if total - largest >= amount - 1 else 0
    given, spare = [largest] + [least] * (amount - 1), total - largest - least * (amount - 1)
    while spare > 0:
        free = [i for i in range(1, amount) if given[i] < largest] or [i for i in range(1, amount) if given[i] < most]
        mass, budget = sum([weights[i] for i in free]), spare
        for i in free:
            addition = min(most - given[i], max(1, budget * weights[i] // mass), spare)
            given[i] = given[i] + addition
            spare = spare - addition
    return np.array(given)


def scatter_about(key, shape, scale, most, cuts=(), held_as=jnp.bfloat16):
    values = scale * jax.random.normal(key, shape, jnp.float32)
    if cuts:
        values = values * block_scale(key, shape, cuts, -0.22, 0.18)
    return jnp.clip(values, -most, most).astype(held_as)


def setup_inputs(seed: int = 0) -> dict:
    key_list = jax.random.split(jax.random.key(seed), 9)
    grad_out = scatter_about(key_list[0], (SECTIONS, MB, TOKENS, D), 1.0, 6.0, ((0, 4), (2, 32)))
    route_weights = jnp.clip(0.1 + 0.5 * jax.random.uniform(key_list[1], (SECTIONS, MB, TOKENS, TOP), jnp.float32) ** block_scale(key_list[1], (SECTIONS, MB, TOKENS, TOP), ((0, 4), (2, 32)), -0.2, 0.2), 0.1, 0.6)
    expert_ids_keys = jax.random.split(jax.random.fold_in(key_list[2], 1), SECTIONS * MB * TOKENS // TOK_DEV)
    expert_ids_turns = jax.random.permutation(jax.random.fold_in(key_list[2], 3), SECTIONS * MB * TOKENS // TOK_DEV)
    expert_ids = jax.vmap(lambda own, number: assign_block(jax.random.fold_in(key_list[2], 2), own, number, TOK_DEV, EXPERTS, TOP, MOST, 2))(expert_ids_keys, expert_ids_turns).reshape((SECTIONS, MB, TOKENS, TOP))
    hot_pos = draw_hot_pos(jax.random.fold_in(key_list[8], 71), 0)
    up_weight = scatter_about(key_list[4], (SECTIONS, EXPERTS, D, FF), D ** -0.5, 0.125, ((0, 4), (1, 32)))
    down_weight = scatter_about(key_list[5], (SECTIONS, EXPERTS, FF, D), FF ** -0.5, 0.21875, ((0, 4), (1, 32)))
    saved_inputs = scatter_about(key_list[6], (SECTIONS, MB, EXPERTS, EXPERTS, SLOTS, D), 1.0, 6.0, ((0, 4), (2, 32)))
    saved_gates = scatter_about(key_list[7], (SECTIONS, MB, EXPERTS, EXPERTS, SLOTS, FF), 1.5, 8.0, ((0, 4), (2, 32)))
    return dict(grad_out=grad_out, route_weights=route_weights, expert_ids=expert_ids, hot_pos=hot_pos, up_weight=up_weight, down_weight=down_weight, saved_inputs=saved_inputs, saved_gates=saved_gates)


def route_slots(expert_row, sender, hot_table, num_experts, most_rows, slot_count):
    onehot = (expert_row[:, None] == jnp.arange(num_experts, dtype=jnp.int32)[None, :]).astype(jnp.int32)
    order_pos = (jnp.sum(jnp.cumsum(onehot, axis=0).astype(jnp.int32) * onehot, axis=1) - 1).astype(jnp.int32)
    group_id = expert_row // REPL
    hot_count = hot_table.shape[0]
    owner_pos = jnp.sum((group_id[:, None] == jnp.arange(hot_count, dtype=jnp.int32)[None, :]).astype(jnp.int32) * hot_table[None, :], axis=1).astype(jnp.int32)
    is_hot = (expert_row % REPL) == owner_pos
    target = jnp.where(is_hot, REPL * group_id + (sender + order_pos) % REPL, expert_row)
    slot_pos = jnp.where(is_hot, most_rows + order_pos // REPL, order_pos)
    return (target * slot_count + slot_pos).astype(jnp.int32)


def expert_rows(grad_rows, input_rows, gate_rows, up_w, down_w):
    up_value = jnp.dot(input_rows, up_w, preferred_element_type=jnp.float32)
    gate_value = gate_rows.astype(jnp.float32)
    gate_sig = jax.nn.sigmoid(gate_value)
    active = gate_value * gate_sig
    hidden = (active * up_value).astype(jnp.bfloat16)
    grad_hidden = lax.dot_general(grad_rows, down_w, (((1,), (1,)), ((), ())), preferred_element_type=jnp.float32)
    grad_up = (grad_hidden * active).astype(jnp.bfloat16)
    grad_gate = (grad_hidden * up_value * gate_sig * (1.0 + gate_value * (1.0 - gate_sig))).astype(jnp.bfloat16)
    back_rows = lax.dot_general(grad_up, up_w, (((1,), (1,)), ((), ())), preferred_element_type=jnp.float32).astype(jnp.bfloat16)
    down_term = lax.dot_general(hidden, grad_rows, (((0,), (0,)), ((), ())), preferred_element_type=jnp.float32)
    up_term = lax.dot_general(input_rows, grad_up, (((0,), (0,)), ((), ())), preferred_element_type=jnp.float32)
    return back_rows, grad_gate, up_term, down_term


def reference(grad_out, route_weights, expert_ids, hot_pos, up_weight, down_weight, saved_inputs, saved_gates):
    features = grad_out.shape[-1]
    hidden_units = saved_gates.shape[-1]
    target_all = jnp.arange(EXPERTS, dtype=jnp.int32)
    token_all, up_all, down_all, gate_all, hot_up_all, hot_down_all = [], [], [], [], [], []
    for section_idx in range(SECTIONS):
        hot_table = hot_pos[section_idx]
        group_of = (target_all // REPL).astype(jnp.int32)
        hot_expert = (REPL * group_of + hot_table[group_of]).astype(jnp.int32)
        up_section = up_weight[section_idx]
        down_section = down_weight[section_idx]
        index_list, arrive_list = [], []
        for batch_idx in range(MB):
            block_ids = expert_ids[section_idx, batch_idx].reshape(EXPERTS, TOK_DEV * TOP)
            flat_index = jax.vmap(lambda block_row, sender: route_slots(block_row, sender, hot_table, EXPERTS, MOST, SLOTS))(block_ids, target_all)
            scaled = (route_weights[section_idx, batch_idx][:, :, None] * grad_out[section_idx, batch_idx][:, None, :].astype(jnp.float32)).astype(jnp.bfloat16)
            scaled = scaled.reshape(EXPERTS, TOK_DEV * TOP, features)
            buffers = jax.vmap(lambda where_to, values: jnp.zeros((EXPERTS * SLOTS, features), jnp.bfloat16).at[where_to].set(values))(flat_index, scaled)
            buffers = buffers.reshape(EXPERTS, EXPERTS, SLOTS, features).transpose(1, 0, 2, 3)
            index_list.append(flat_index)
            arrive_list.append(buffers)
        received = jnp.stack(arrive_list, 1)
        inputs_section = saved_inputs[section_idx].transpose(1, 0, 2, 3, 4)
        gates_section = saved_gates[section_idx].transpose(1, 0, 2, 3, 4)

        def per_device(packed):
            device, arrived, inputs_dev, gates_dev = packed
            own_up = up_section[device]
            own_down = down_section[device]
            hot_up = up_section[hot_expert[device]]
            hot_down = down_section[hot_expert[device]]
            own_up_sum = jnp.zeros((features, hidden_units), jnp.float32)
            own_down_sum = jnp.zeros((hidden_units, features), jnp.float32)
            rep_up_sum = jnp.zeros((features, hidden_units), jnp.float32)
            rep_down_sum = jnp.zeros((hidden_units, features), jnp.float32)
            back_list, gate_list = [], []
            for batch_idx in range(MB):
                first_part = expert_rows(arrived[batch_idx][:, :MOST].reshape(-1, features), inputs_dev[batch_idx][:, :MOST].reshape(-1, features), gates_dev[batch_idx][:, :MOST].reshape(-1, hidden_units), own_up, own_down)
                second = expert_rows(arrived[batch_idx][:, MOST:].reshape(-1, features), inputs_dev[batch_idx][:, MOST:].reshape(-1, features), gates_dev[batch_idx][:, MOST:].reshape(-1, hidden_units), hot_up, hot_down)
                back_list.append(jnp.concatenate([first_part[0].reshape(EXPERTS, MOST, features), second[0].reshape(EXPERTS, SLOTS - MOST, features)], 1))
                gate_list.append(jnp.concatenate([first_part[1].reshape(EXPERTS, MOST, hidden_units), second[1].reshape(EXPERTS, SLOTS - MOST, hidden_units)], 1))
                own_up_sum = own_up_sum + first_part[2]
                own_down_sum = own_down_sum + first_part[3]
                rep_up_sum = rep_up_sum + second[2]
                rep_down_sum = rep_down_sum + second[3]
            return (jnp.stack(back_list, 0), jnp.stack(gate_list, 0), own_up_sum.astype(jnp.bfloat16), own_down_sum.astype(jnp.bfloat16), rep_up_sum.astype(jnp.bfloat16), rep_down_sum.astype(jnp.bfloat16))

        backs, gate_grads, own_up_all, own_down_all, rep_up_all, rep_down_all = lax.map(per_device, (target_all, received, inputs_section, gates_section))
        group_up = jnp.sum(rep_up_all.reshape(HOT, REPL, features, hidden_units).astype(jnp.float32), axis=1).astype(jnp.bfloat16)
        group_down = jnp.sum(rep_down_all.reshape(HOT, REPL, hidden_units, features).astype(jnp.float32), axis=1).astype(jnp.bfloat16)
        hot_up_all.append(group_up.reshape(EXPERTS, features // REPL, hidden_units))
        hot_down_all.append(group_down.reshape(EXPERTS, hidden_units // REPL, features))
        up_all.append(own_up_all)
        down_all.append(own_down_all)
        gate_all.append(gate_grads.transpose(1, 0, 2, 3, 4))
        batch_grads = []
        for batch_idx in range(MB):
            flat_back = backs[:, batch_idx].transpose(1, 0, 2, 3).reshape(EXPERTS, EXPERTS * SLOTS, features)
            gathered = jnp.take_along_axis(flat_back, index_list[batch_idx][:, :, None], axis=1)
            summed = jnp.sum(gathered.reshape(TOKENS, TOP, features).astype(jnp.float32), axis=1)
            batch_grads.append((summed + grad_out[section_idx, batch_idx].astype(jnp.float32)).astype(jnp.bfloat16))
        token_all.append(jnp.stack(batch_grads, 0))
    sent_back = jnp.roll(jnp.stack(token_all, 0), -1, axis=0)
    return sent_back, jnp.stack(up_all, 0), jnp.stack(down_all, 0), jnp.stack(gate_all, 0), jnp.stack(hot_up_all, 0), jnp.stack(hot_down_all, 0)
```

```python
import jax
import jax.numpy as jnp
from jax import lax
from jax.sharding import PartitionSpec as P

TOP = 8
REPL = 4
MB = 2


def partner(value, axis, bit):
    mask = 2**bit
    pairs = [(source, source ^ mask) for source in range(lax.axis_size(axis))]
    return lax.ppermute(value, axis, pairs)


def from_behind(block, axis, distance):
    devices = range(lax.axis_size(axis))
    route = [((i - distance) % len(devices), i) for i in devices]
    return lax.ppermute(block, axis, route)


def route_slots(expert_row, sender, hot_table, num_experts, most_rows, slot_count):
    onehot = (expert_row[:, None] == jnp.arange(num_experts, dtype=jnp.int32)[None, :]).astype(
        jnp.int32
    )
    order_pos = jnp.sum(jnp.cumsum(onehot, axis=0) * onehot, axis=1) - 1
    group_id = expert_row // REPL
    hot_count = hot_table.shape[0]
    owner_pos = jnp.sum(
        (group_id[:, None] == jnp.arange(hot_count, dtype=jnp.int32)[None, :]).astype(jnp.int32)
        * hot_table[None, :],
        axis=1,
    )
    is_hot = expert_row % REPL == owner_pos
    target = jnp.where(is_hot, REPL * group_id + (sender + order_pos) % REPL, expert_row)
    slot_pos = jnp.where(is_hot, most_rows + order_pos // REPL, order_pos)
    return target * slot_count + slot_pos


def expert_rows(grad_rows, input_rows, gate_rows, up_w, down_w):
    up_value = jnp.dot(input_rows, up_w, preferred_element_type=jnp.float32)
    gate_value = gate_rows.astype(jnp.float32)
    gate_sig = jax.nn.sigmoid(gate_value)
    active = gate_value * gate_sig
    hidden = (active * up_value).astype(jnp.bfloat16)
    grad_hidden = lax.dot_general(
        grad_rows, down_w, (((1,), (1,)), ((), ())), preferred_element_type=jnp.float32
    )
    grad_up = (grad_hidden * active).astype(jnp.bfloat16)
    grad_gate = (grad_hidden * up_value * gate_sig * (1.0 + gate_value * (1.0 - gate_sig))).astype(
        jnp.bfloat16
    )
    back_rows = lax.dot_general(
        grad_up, up_w, (((1,), (1,)), ((), ())), preferred_element_type=jnp.float32
    ).astype(jnp.bfloat16)
    down_term = lax.dot_general(
        hidden, grad_rows, (((0,), (0,)), ((), ())), preferred_element_type=jnp.float32
    )
    up_term = lax.dot_general(
        input_rows, grad_up, (((0,), (0,)), ((), ())), preferred_element_type=jnp.float32
    )
    return (back_rows, grad_gate, up_term, down_term)


def take_part(matrix, index, parts):
    length = matrix.shape[0] // parts
    return lax.dynamic_slice_in_dim(matrix, index * length, length, 0)


def per_device(
    grad_out, route_weights, expert_ids, hot_pos, up_weight, down_weight, saved_inputs, saved_gates
):
    experts = lax.axis_size("grp") * lax.axis_size("j")
    device = lax.axis_index("grp") * lax.axis_size("j") + lax.axis_index("j")
    features = grad_out.shape[-1]
    hidden_units = saved_gates.shape[-1]
    token_count = grad_out.shape[2]
    slot_count = saved_inputs.shape[4]
    quarter_rows = slot_count // (REPL + 1)
    most_rows = REPL * quarter_rows
    hot_table = hot_pos[0]
    group_id = device // REPL
    local_pos = device % REPL
    owner_pos = jnp.sum(
        jnp.where(jnp.arange(hot_table.shape[0], dtype=jnp.int32) == group_id, hot_table, 0)
    )
    is_owner = local_pos == owner_pos
    own_up = up_weight[0, 0]
    own_down = down_weight[0, 0]
    owner_mask = is_owner.astype(jnp.bfloat16)
    hot_up, hot_down = lax.psum((own_up * owner_mask, own_down * owner_mask), "j")
    outputs = []
    token_grads = []
    for batch_idx in range(MB):
        expert_row = expert_ids[0, batch_idx].reshape(-1)
        token_flat_index = route_slots(
            expert_row, device, hot_table, experts, most_rows, slot_count
        )
        scaled = (
            route_weights[0, batch_idx][:, :, None]
            * grad_out[0, batch_idx][:, None, :].astype(jnp.float32)
        ).astype(jnp.bfloat16)
        routed_rows = scaled.reshape(-1, features)
        buffer = (
            jnp.zeros((experts * slot_count, features), jnp.bfloat16)
            .at[token_flat_index]
            .set(routed_rows)
        )
        flat_index, buffer = (token_flat_index, buffer.reshape(experts, slot_count, features))
        received = lax.all_to_all(buffer, ("grp", "j"), split_axis=0, concat_axis=0, tiled=True)
        inputs_batch = saved_inputs[0, batch_idx, 0]
        gates_batch = saved_gates[0, batch_idx, 0]
        first_part = expert_rows(
            received[:, :most_rows].reshape(-1, features),
            inputs_batch[:, :most_rows].reshape(-1, features),
            gates_batch[:, :most_rows].reshape(-1, hidden_units),
            own_up,
            own_down,
        )
        expert_second = expert_rows(
            received[:, most_rows:].reshape(-1, features),
            inputs_batch[:, most_rows:].reshape(-1, features),
            gates_batch[:, most_rows:].reshape(-1, hidden_units),
            hot_up,
            hot_down,
        )
        back = jnp.concatenate(
            [
                first_part[0].reshape(experts, most_rows, features),
                expert_second[0].reshape(experts, quarter_rows, features),
            ],
            1,
        )
        gate_grad = jnp.concatenate(
            [
                first_part[1].reshape(experts, most_rows, hidden_units),
                expert_second[1].reshape(experts, quarter_rows, hidden_units),
            ],
            1,
        )
        results = (
            back,
            gate_grad,
            first_part[2],
            first_part[3],
            expert_second[2],
            expert_second[3],
        )
        outputs.append(results)
        returned = lax.all_to_all(results[0], ("grp", "j"), split_axis=0, concat_axis=0, tiled=True)
        gathered = returned.reshape(experts * slot_count, features)[flat_index]
        summed = jnp.sum(gathered.reshape(token_count, TOP, features).astype(jnp.float32), axis=1)
        token_grads.append(
            (summed + grad_out[0, batch_idx].astype(jnp.float32)).astype(jnp.bfloat16)
        )
    own_up_sum = jnp.zeros((features, hidden_units), jnp.float32)
    own_down_sum = jnp.zeros((hidden_units, features), jnp.float32)
    rep_up_sum = jnp.zeros((features, hidden_units), jnp.float32)
    rep_down_sum = jnp.zeros((hidden_units, features), jnp.float32)
    for member in outputs:
        own_up_sum = own_up_sum + member[2]
        own_down_sum = own_down_sum + member[3]
        rep_up_sum = rep_up_sum + member[4]
        rep_down_sum = rep_down_sum + member[5]
    sent_back = from_behind(jnp.stack(token_grads, 0), "pipe", -1)
    rep_terms = (
        rep_up_sum.astype(jnp.bfloat16).astype(jnp.float32),
        rep_down_sum.astype(jnp.bfloat16).astype(jnp.float32),
    )
    hot_up_part, hot_down_part = lax.psum_scatter(rep_terms, "j", scatter_dimension=0, tiled=True)
    hot_up_part = hot_up_part.astype(jnp.bfloat16)
    hot_down_part = hot_down_part.astype(jnp.bfloat16)
    up_grad = own_up_sum.astype(jnp.bfloat16)
    down_grad = own_down_sum.astype(jnp.bfloat16)
    gate_grads = jnp.stack([member[1] for member in outputs], 0)
    return (
        sent_back[None],
        up_grad[None, None],
        down_grad[None, None],
        gate_grads[None, :, None],
        hot_up_part[None, None],
        hot_down_part[None, None],
    )


EXPERT = ("grp", "j")


def solution(mesh):
    groups = mesh.devices.reshape(mesh.shape["pipe"], -1, REPL)
    group_mesh = jax.sharding.Mesh(groups, ("pipe", "grp", "j"))
    return jax.shard_map(
        per_device,
        mesh=group_mesh,
        in_specs=(
            P("pipe", None, EXPERT, None),
            P("pipe", None, EXPERT, None),
            P("pipe", None, EXPERT, None),
            P("pipe", None),
            P("pipe", EXPERT, None, None),
            P("pipe", EXPERT, None, None),
            P("pipe", None, EXPERT, None, None, None),
            P("pipe", None, EXPERT, None, None, None),
        ),
        out_specs=(
            P("pipe", None, EXPERT, None),
            P("pipe", EXPERT, None, None),
            P("pipe", EXPERT, None, None),
            P("pipe", None, EXPERT, None, None, None),
            P("pipe", EXPERT, None, None),
            P("pipe", EXPERT, None, None),
        ),
        check_vma=False,
    )
```

```python
import jax
import jax.numpy as jnp
from jax import lax
from jax.sharding import PartitionSpec as P

TOP = 8
REPL = 4
MB = 2


def partner(value, axis, bit):
    mask = 2**bit
    pairs = [(source, source ^ mask) for source in range(lax.axis_size(axis))]
    return lax.ppermute(value, axis, pairs)


def from_behind(block, axis, distance):
    devices = range(lax.axis_size(axis))
    route = [((i - distance) % len(devices), i) for i in devices]
    return lax.ppermute(block, axis, route)


def shift(value, distance):
    count = lax.axis_size("j")
    return lax.ppermute(value, "j", [(k, (k + distance) % count) for k in range(count)])


def quarter(matrix, index, pieces=REPL):
    length = matrix.shape[0] // pieces
    return lax.dynamic_slice_in_dim(matrix, index * length, length, 0)


def group_reduce_scatter(terms, local_pos):
    def parts(offset):
        return [quarter(t, (local_pos + offset) % REPL) for t in terms]

    def half(matrix, which):
        length = matrix.shape[0] // 2
        return matrix[which * length:(which + 1) * length]

    right_next, right_far = parts(1), parts(2)
    left_next = parts(3)
    to_right = [jnp.concatenate([a, half(b, 0)], 0) for a, b in zip(right_next, right_far)]
    to_left = [jnp.concatenate([a, half(b, 1)], 0) for a, b in zip(left_next, right_far)]
    from_left = shift(to_right, 1)
    from_right = shift(to_left, -1)
    sizes = [t.shape[0] // REPL for t in terms]
    relay_right = [m[n:] for m, n in zip(from_left, sizes)]
    relay_left = [m[n:] for m, n in zip(from_right, sizes)]
    far_first = shift(relay_right, 1)
    far_second = shift(relay_left, -1)
    mine = parts(0)
    sums = []
    for k, n in enumerate(sizes):
        total = (
            mine[k].astype(jnp.float32)
            + from_left[k][:n].astype(jnp.float32)
            + from_right[k][:n].astype(jnp.float32)
            + jnp.concatenate([far_first[k], far_second[k]], 0).astype(jnp.float32)
        )
        sums.append(total)
    return sums


def route_slots(expert_row, sender, hot_table, num_experts, most_rows, slot_count):
    onehot = (expert_row[:, None] == jnp.arange(num_experts, dtype=jnp.int32)[None, :]).astype(
        jnp.int32
    )
    order_pos = jnp.sum(jnp.cumsum(onehot, axis=0) * onehot, axis=1) - 1
    group_id = expert_row // REPL
    hot_count = hot_table.shape[0]
    owner_pos = jnp.sum(
        (group_id[:, None] == jnp.arange(hot_count, dtype=jnp.int32)[None, :]).astype(jnp.int32)
        * hot_table[None, :],
        axis=1,
    )
    is_hot = expert_row % REPL == owner_pos
    target = jnp.where(is_hot, REPL * group_id + (sender + order_pos) % REPL, expert_row)
    slot_pos = jnp.where(is_hot, most_rows + order_pos // REPL, order_pos)
    quarter_rows = slot_count - most_rows
    own_index = target * most_rows + slot_pos
    hot_index = num_experts * most_rows + target * quarter_rows + (slot_pos - most_rows)
    return jnp.where(is_hot, hot_index, own_index)


def expert_rows(grad_rows, input_rows, gate_rows, up_w, down_w):
    up_value = jnp.dot(input_rows, up_w, preferred_element_type=jnp.float32)
    gate_value = gate_rows.astype(jnp.float32)
    gate_sig = jax.nn.sigmoid(gate_value)
    active = gate_value * gate_sig
    hidden = (active * up_value).astype(jnp.bfloat16)
    grad_hidden = lax.dot_general(
        grad_rows, down_w, (((1,), (1,)), ((), ())), preferred_element_type=jnp.float32
    )
    grad_up = (grad_hidden * active).astype(jnp.bfloat16)
    grad_gate = (grad_hidden * up_value * gate_sig * (1.0 + gate_value * (1.0 - gate_sig))).astype(
        jnp.bfloat16
    )
    back_rows = lax.dot_general(
        grad_up, up_w, (((1,), (1,)), ((), ())), preferred_element_type=jnp.float32
    ).astype(jnp.bfloat16)
    down_term = lax.dot_general(
        hidden, grad_rows, (((0,), (0,)), ((), ())), preferred_element_type=jnp.float32
    )
    up_term = lax.dot_general(
        input_rows, grad_up, (((0,), (0,)), ((), ())), preferred_element_type=jnp.float32
    )
    return (back_rows, grad_gate, up_term, down_term)


def take_part(matrix, index, parts):
    length = matrix.shape[0] // parts
    return lax.dynamic_slice_in_dim(matrix, index * length, length, 0)


def per_device(
    grad_out, route_weights, expert_ids, hot_pos, up_weight, down_weight, saved_inputs, saved_gates
):
    experts = lax.axis_size("grp") * lax.axis_size("j")
    device = lax.axis_index("grp") * lax.axis_size("j") + lax.axis_index("j")
    features = grad_out.shape[-1]
    hidden_units = saved_gates.shape[-1]
    token_count = grad_out.shape[2]
    slot_count = saved_inputs.shape[4]
    quarter_rows = slot_count // (REPL + 1)
    most_rows = REPL * quarter_rows
    hot_table = hot_pos[0]
    group_id = device // REPL
    local_pos = device % REPL
    owner_pos = jnp.sum(
        jnp.where(jnp.arange(hot_table.shape[0], dtype=jnp.int32) == group_id, hot_table, 0)
    )
    is_owner = local_pos == owner_pos
    own_up = up_weight[0, 0]
    own_down = down_weight[0, 0]
    owner_mask = is_owner.astype(jnp.bfloat16)
    hot_up, hot_down = lax.psum((own_up * owner_mask, own_down * owner_mask), "j")
    outputs = []
    token_grads = []
    for batch_idx in range(MB):
        expert_row = expert_ids[0, batch_idx].reshape(-1)
        token_flat_index = route_slots(
            expert_row, device, hot_table, experts, most_rows, slot_count
        )
        scaled = (
            route_weights[0, batch_idx][:, :, None]
            * grad_out[0, batch_idx][:, None, :].astype(jnp.float32)
        ).astype(jnp.bfloat16)
        routed_rows = scaled.reshape(-1, features)
        buffer = (
            jnp.zeros((experts * slot_count, features), jnp.bfloat16)
            .at[token_flat_index]
            .set(routed_rows)
        )
        own_rows = experts * most_rows
        received_own = lax.all_to_all(
            buffer[:own_rows], EXPERT, split_axis=0, concat_axis=0, tiled=True
        )
        received_hot = lax.all_to_all(
            buffer[own_rows:], EXPERT, split_axis=0, concat_axis=0, tiled=True
        )
        inputs_batch = saved_inputs[0, batch_idx, 0]
        gates_batch = saved_gates[0, batch_idx, 0]
        first_part = expert_rows(
            received_own,
            inputs_batch[:, :most_rows].reshape(-1, features),
            gates_batch[:, :most_rows].reshape(-1, hidden_units),
            own_up,
            own_down,
        )
        expert_second = expert_rows(
            received_hot,
            inputs_batch[:, most_rows:].reshape(-1, features),
            gates_batch[:, most_rows:].reshape(-1, hidden_units),
            hot_up,
            hot_down,
        )
        gate_grad = jnp.concatenate(
            [
                first_part[1].reshape(experts, most_rows, hidden_units),
                expert_second[1].reshape(experts, quarter_rows, hidden_units),
            ],
            1,
        )
        outputs.append(
            (None, gate_grad, first_part[2], first_part[3], expert_second[2], expert_second[3])
        )
        returned_own = lax.all_to_all(
            first_part[0], EXPERT, split_axis=0, concat_axis=0, tiled=True
        )
        returned_hot = lax.all_to_all(
            expert_second[0], EXPERT, split_axis=0, concat_axis=0, tiled=True
        )
        returned = jnp.concatenate([returned_own, returned_hot], 0)
        gathered = returned[token_flat_index]
        summed = jnp.sum(gathered.reshape(token_count, TOP, features).astype(jnp.float32), axis=1)
        token_grad = (summed + grad_out[0, batch_idx].astype(jnp.float32)).astype(jnp.bfloat16)
        token_grads.append(from_behind(token_grad, "pipe", -1))
    own_up_sum = jnp.zeros((features, hidden_units), jnp.float32)
    own_down_sum = jnp.zeros((hidden_units, features), jnp.float32)
    rep_up_sum = jnp.zeros((features, hidden_units), jnp.float32)
    rep_down_sum = jnp.zeros((hidden_units, features), jnp.float32)
    for member in outputs:
        own_up_sum = own_up_sum + member[2]
        own_down_sum = own_down_sum + member[3]
        rep_up_sum = rep_up_sum + member[4]
        rep_down_sum = rep_down_sum + member[5]
    sent_back = jnp.stack(token_grads, 0)
    hot_up_part, hot_down_part = group_reduce_scatter(
        (rep_up_sum.astype(jnp.bfloat16), rep_down_sum.astype(jnp.bfloat16)), local_pos
    )
    hot_up_part = hot_up_part.astype(jnp.bfloat16)
    hot_down_part = hot_down_part.astype(jnp.bfloat16)
    up_grad = own_up_sum.astype(jnp.bfloat16)
    down_grad = own_down_sum.astype(jnp.bfloat16)
    gate_grads = jnp.stack([member[1] for member in outputs], 0)
    return (
        sent_back[None],
        up_grad[None, None],
        down_grad[None, None],
        gate_grads[None, :, None],
        hot_up_part[None, None],
        hot_down_part[None, None],
    )


EXPERT = ("grp", "j")


def solution(mesh):
    groups = mesh.devices.reshape(mesh.shape["pipe"], -1, REPL)
    group_mesh = jax.sharding.Mesh(groups, ("pipe", "grp", "j"))
    return jax.shard_map(
        per_device,
        mesh=group_mesh,
        in_specs=(
            P("pipe", None, EXPERT, None),
            P("pipe", None, EXPERT, None),
            P("pipe", None, EXPERT, None),
            P("pipe", None),
            P("pipe", EXPERT, None, None),
            P("pipe", EXPERT, None, None),
            P("pipe", None, EXPERT, None, None, None),
            P("pipe", None, EXPERT, None, None, None),
        ),
        out_specs=(
            P("pipe", None, EXPERT, None),
            P("pipe", EXPERT, None, None),
            P("pipe", EXPERT, None, None),
            P("pipe", None, EXPERT, None, None, None),
            P("pipe", EXPERT, None, None),
            P("pipe", EXPERT, None, None),
        ),
        check_vma=False,
    )
```

```python
import jax
import numpy as np
import jax.numpy as jnp
from jax import lax
from jax.sharding import PartitionSpec as P

TOP = 8
REPL = 4
MB = 2


def partner(value, axis, bit):
    mask = 2**bit
    pairs = [(source, source ^ mask) for source in range(lax.axis_size(axis))]
    return lax.ppermute(value, axis, pairs)


def from_behind(block, axis, distance):
    devices = range(lax.axis_size(axis))
    route = [((i - distance) % len(devices), i) for i in devices]
    return lax.ppermute(block, axis, route)


def shift(value, distance):
    count = lax.axis_size("j")
    return lax.ppermute(value, "j", [(k, (k + distance) % count) for k in range(count)])


def quarter(matrix, index, pieces=REPL):
    length = matrix.shape[0] // pieces
    return lax.dynamic_slice_in_dim(matrix, index * length, length, 0)


def group_reduce_scatter(terms, local_pos):
    def parts(offset):
        return [quarter(t, (local_pos + offset) % REPL) for t in terms]

    def half(matrix, which):
        length = matrix.shape[0] // 2
        return matrix[which * length:(which + 1) * length]

    right_next, right_far = parts(1), parts(2)
    left_next = parts(3)
    to_right = [jnp.concatenate([a, half(b, 0)], 0) for a, b in zip(right_next, right_far)]
    to_left = [jnp.concatenate([a, half(b, 1)], 0) for a, b in zip(left_next, right_far)]
    from_left = shift(to_right, 1)
    from_right = shift(to_left, -1)
    sizes = [t.shape[0] // REPL for t in terms]
    relay_right = [m[n:] for m, n in zip(from_left, sizes)]
    relay_left = [m[n:] for m, n in zip(from_right, sizes)]
    far_first = shift(relay_right, 1)
    far_second = shift(relay_left, -1)
    mine = parts(0)
    sums = []
    for k, n in enumerate(sizes):
        total = (
            mine[k].astype(jnp.float32)
            + from_left[k][:n].astype(jnp.float32)
            + from_right[k][:n].astype(jnp.float32)
            + jnp.concatenate([far_first[k], far_second[k]], 0).astype(jnp.float32)
        )
        sums.append(total)
    return sums


def slot_orders(experts, most_rows, slot_count):
    quarter_rows = slot_count - most_rows
    senders = np.concatenate(
        [np.repeat(np.arange(experts), most_rows), np.repeat(np.arange(experts), quarter_rows)]
    ).astype(np.int32)
    slots = np.concatenate(
        [np.tile(np.arange(most_rows), experts), most_rows + np.tile(np.arange(quarter_rows), experts)]
    ).astype(np.int32)
    sender_ix = np.arange(experts)[:, None]
    slot_ix = np.arange(slot_count)[None, :]
    inverse = np.where(
        slot_ix < most_rows,
        sender_ix * most_rows + slot_ix,
        experts * most_rows + sender_ix * quarter_rows + slot_ix - most_rows,
    ).astype(np.int32)
    return senders, slots, inverse


def route_slots(expert_row, sender, hot_table, num_experts, most_rows, slot_count):
    onehot = (expert_row[:, None] == jnp.arange(num_experts, dtype=jnp.int32)[None, :]).astype(
        jnp.int32
    )
    order_pos = jnp.sum(jnp.cumsum(onehot, axis=0) * onehot, axis=1) - 1
    group_id = expert_row // REPL
    hot_count = hot_table.shape[0]
    owner_pos = jnp.sum(
        (group_id[:, None] == jnp.arange(hot_count, dtype=jnp.int32)[None, :]).astype(jnp.int32)
        * hot_table[None, :],
        axis=1,
    )
    is_hot = expert_row % REPL == owner_pos
    target = jnp.where(is_hot, REPL * group_id + (sender + order_pos) % REPL, expert_row)
    slot_pos = jnp.where(is_hot, most_rows + order_pos // REPL, order_pos)
    return target, slot_pos


def expert_rows(grad_rows, input_rows, gate_rows, up_w, down_w):
    up_value = jnp.dot(input_rows, up_w, preferred_element_type=jnp.float32)
    gate_value = gate_rows.astype(jnp.float32)
    gate_sig = jax.nn.sigmoid(gate_value)
    active = gate_value * gate_sig
    hidden = (active * up_value).astype(jnp.bfloat16)
    grad_hidden = lax.dot_general(
        grad_rows, down_w, (((1,), (1,)), ((), ())), preferred_element_type=jnp.float32
    )
    grad_up = (grad_hidden * active).astype(jnp.bfloat16)
    grad_gate = (grad_hidden * up_value * gate_sig * (1.0 + gate_value * (1.0 - gate_sig))).astype(
        jnp.bfloat16
    )
    back_rows = lax.dot_general(
        grad_up, up_w, (((1,), (1,)), ((), ())), preferred_element_type=jnp.float32
    ).astype(jnp.bfloat16)
    down_term = lax.dot_general(
        hidden, grad_rows, (((0,), (0,)), ((), ())), preferred_element_type=jnp.float32
    )
    up_term = lax.dot_general(
        input_rows, grad_up, (((0,), (0,)), ((), ())), preferred_element_type=jnp.float32
    )
    return (back_rows, grad_gate, up_term, down_term)


def take_part(matrix, index, parts):
    length = matrix.shape[0] // parts
    return lax.dynamic_slice_in_dim(matrix, index * length, length, 0)


def per_device(
    grad_out, route_weights, expert_ids, hot_pos, up_weight, down_weight, saved_inputs, saved_gates
):
    experts = lax.axis_size("grp") * lax.axis_size("j")
    device = lax.axis_index("grp") * lax.axis_size("j") + lax.axis_index("j")
    features = grad_out.shape[-1]
    hidden_units = saved_gates.shape[-1]
    token_count = grad_out.shape[2]
    slot_count = saved_inputs.shape[4]
    quarter_rows = slot_count // (REPL + 1)
    most_rows = REPL * quarter_rows
    hot_table = hot_pos[0]
    group_id = device // REPL
    local_pos = device % REPL
    owner_pos = jnp.sum(
        jnp.where(jnp.arange(hot_table.shape[0], dtype=jnp.int32) == group_id, hot_table, 0)
    )
    is_owner = local_pos == owner_pos
    own_up = up_weight[0, 0]
    own_down = down_weight[0, 0]
    owner_mask = is_owner.astype(jnp.bfloat16)
    hot_up, hot_down = lax.psum((own_up * owner_mask, own_down * owner_mask), "j")
    outputs = []
    token_grads = []
    senders, slots, inverse = slot_orders(experts, most_rows, slot_count)
    own_rows = experts * most_rows

    def by_part(array):
        return array[senders, slots]

    for batch_idx in range(MB):
        expert_row = expert_ids[0, batch_idx].reshape(-1)
        target, slot_pos = route_slots(
            expert_row, device, hot_table, experts, most_rows, slot_count
        )
        scaled = (
            route_weights[0, batch_idx][:, :, None]
            * grad_out[0, batch_idx][:, None, :].astype(jnp.float32)
        ).astype(jnp.bfloat16)
        routed_rows = scaled.reshape(-1, features)
        buffer = (
            jnp.zeros((experts, slot_count, features), jnp.bfloat16)
            .at[target, slot_pos]
            .set(routed_rows)
        )
        received = by_part(lax.all_to_all(buffer, EXPERT, split_axis=0, concat_axis=0, tiled=True))
        inputs_rows = by_part(saved_inputs[0, batch_idx, 0])
        gates_rows = by_part(saved_gates[0, batch_idx, 0])
        first_part = expert_rows(
            received[:own_rows], inputs_rows[:own_rows], gates_rows[:own_rows], own_up, own_down
        )
        expert_second = expert_rows(
            received[own_rows:], inputs_rows[own_rows:], gates_rows[own_rows:], hot_up, hot_down
        )
        back = jnp.concatenate([first_part[0], expert_second[0]], 0)[inverse]
        gate_grad = jnp.concatenate([first_part[1], expert_second[1]], 0)[inverse]
        outputs.append(
            (None, gate_grad, first_part[2], first_part[3], expert_second[2], expert_second[3])
        )
        returned = lax.all_to_all(back, EXPERT, split_axis=0, concat_axis=0, tiled=True)
        gathered = returned[target, slot_pos]
        summed = jnp.sum(gathered.reshape(token_count, TOP, features).astype(jnp.float32), axis=1)
        token_grad = (summed + grad_out[0, batch_idx].astype(jnp.float32)).astype(jnp.bfloat16)
        token_grads.append(from_behind(token_grad, "pipe", -1))
    own_up_sum = jnp.zeros((features, hidden_units), jnp.float32)
    own_down_sum = jnp.zeros((hidden_units, features), jnp.float32)
    rep_up_sum = jnp.zeros((features, hidden_units), jnp.float32)
    rep_down_sum = jnp.zeros((hidden_units, features), jnp.float32)
    for member in outputs:
        own_up_sum = own_up_sum + member[2]
        own_down_sum = own_down_sum + member[3]
        rep_up_sum = rep_up_sum + member[4]
        rep_down_sum = rep_down_sum + member[5]
    sent_back = jnp.stack(token_grads, 0)
    hot_up_part, hot_down_part = group_reduce_scatter(
        (rep_up_sum.astype(jnp.bfloat16), rep_down_sum.astype(jnp.bfloat16)), local_pos
    )
    hot_up_part = hot_up_part.astype(jnp.bfloat16)
    hot_down_part = hot_down_part.astype(jnp.bfloat16)
    up_grad = own_up_sum.astype(jnp.bfloat16)
    down_grad = own_down_sum.astype(jnp.bfloat16)
    gate_grads = jnp.stack([member[1] for member in outputs], 0)
    return (
        sent_back[None],
        up_grad[None, None],
        down_grad[None, None],
        gate_grads[None, :, None],
        hot_up_part[None, None],
        hot_down_part[None, None],
    )


EXPERT = ("grp", "j")


def solution(mesh):
    groups = mesh.devices.reshape(mesh.shape["pipe"], -1, REPL)
    group_mesh = jax.sharding.Mesh(groups, ("pipe", "grp", "j"))
    return jax.shard_map(
        per_device,
        mesh=group_mesh,
        in_specs=(
            P("pipe", None, EXPERT, None),
            P("pipe", None, EXPERT, None),
            P("pipe", None, EXPERT, None),
            P("pipe", None),
            P("pipe", EXPERT, None, None),
            P("pipe", EXPERT, None, None),
            P("pipe", None, EXPERT, None, None, None),
            P("pipe", None, EXPERT, None, None, None),
        ),
        out_specs=(
            P("pipe", None, EXPERT, None),
            P("pipe", EXPERT, None, None),
            P("pipe", EXPERT, None, None),
            P("pipe", None, EXPERT, None, None, None),
            P("pipe", EXPERT, None, None),
            P("pipe", EXPERT, None, None),
        ),
        check_vma=False,
    )
```

```python
import jax
import jax.numpy as jnp
from jax import lax
from jax.sharding import PartitionSpec as P

TOP = 8
REPL = 4
MB = 2


def partner(value, axis, bit):
    mask = 2**bit
    pairs = [(source, source ^ mask) for source in range(lax.axis_size(axis))]
    return lax.ppermute(value, axis, pairs)


def from_behind(block, axis, distance):
    devices = range(lax.axis_size(axis))
    route = [((i - distance) % len(devices), i) for i in devices]
    return lax.ppermute(block, axis, route)


def shift(value, distance):
    count = lax.axis_size("j")
    return lax.ppermute(value, "j", [(k, (k + distance) % count) for k in range(count)])


def quarter(matrix, index, pieces=REPL):
    length = matrix.shape[0] // pieces
    return lax.dynamic_slice_in_dim(matrix, index * length, length, 0)


def group_reduce_scatter(terms, local_pos):
    def parts(offset):
        return [quarter(t, (local_pos + offset) % REPL) for t in terms]

    def half(matrix, which):
        length = matrix.shape[0] // 2
        return matrix[which * length:(which + 1) * length]

    right_next, right_far = parts(1), parts(2)
    left_next = parts(3)
    to_right = [jnp.concatenate([a, half(b, 0)], 0) for a, b in zip(right_next, right_far)]
    to_left = [jnp.concatenate([a, half(b, 1)], 0) for a, b in zip(left_next, right_far)]
    from_left = shift(to_right, 1)
    from_right = shift(to_left, -1)
    sizes = [t.shape[0] // REPL for t in terms]
    relay_right = [m[n:] for m, n in zip(from_left, sizes)]
    relay_left = [m[n:] for m, n in zip(from_right, sizes)]
    far_first = shift(relay_right, 1)
    far_second = shift(relay_left, -1)
    mine = parts(0)
    sums = []
    for k, n in enumerate(sizes):
        total = (
            mine[k].astype(jnp.float32)
            + from_left[k][:n].astype(jnp.float32)
            + from_right[k][:n].astype(jnp.float32)
            + jnp.concatenate([far_first[k], far_second[k]], 0).astype(jnp.float32)
        )
        sums.append(total)
    return sums


def route_slots(expert_row, sender, hot_table, num_experts, most_rows, slot_count):
    onehot = (expert_row[:, None] == jnp.arange(num_experts, dtype=jnp.int32)[None, :]).astype(
        jnp.int32
    )
    order_pos = jnp.sum(jnp.cumsum(onehot, axis=0) * onehot, axis=1) - 1
    group_id = expert_row // REPL
    hot_count = hot_table.shape[0]
    owner_pos = jnp.sum(
        (group_id[:, None] == jnp.arange(hot_count, dtype=jnp.int32)[None, :]).astype(jnp.int32)
        * hot_table[None, :],
        axis=1,
    )
    is_hot = expert_row % REPL == owner_pos
    target = jnp.where(is_hot, REPL * group_id + (sender + order_pos) % REPL, expert_row)
    slot_pos = jnp.where(is_hot, most_rows + order_pos // REPL, order_pos)
    return target * slot_count + slot_pos


def expert_rows(grad_rows, input_rows, gate_rows, up_w, down_w):
    up_value = jnp.einsum("isd,df->isf", input_rows, up_w, preferred_element_type=jnp.float32)
    gate_value = gate_rows.astype(jnp.float32)
    gate_sig = jax.nn.sigmoid(gate_value)
    active = gate_value * gate_sig
    hidden = (active * up_value).astype(jnp.bfloat16)
    grad_hidden = jnp.einsum("isd,fd->isf", grad_rows, down_w, preferred_element_type=jnp.float32)
    grad_up = (grad_hidden * active).astype(jnp.bfloat16)
    grad_gate = (grad_hidden * up_value * gate_sig * (1.0 + gate_value * (1.0 - gate_sig))).astype(
        jnp.bfloat16
    )
    back_rows = jnp.einsum("isf,df->isd", grad_up, up_w, preferred_element_type=jnp.float32).astype(
        jnp.bfloat16
    )
    down_term = jnp.einsum("isf,isd->fd", hidden, grad_rows, preferred_element_type=jnp.float32)
    up_term = jnp.einsum("isd,isf->df", input_rows, grad_up, preferred_element_type=jnp.float32)
    return (back_rows, grad_gate, up_term, down_term)


def take_part(matrix, index, parts):
    length = matrix.shape[0] // parts
    return lax.dynamic_slice_in_dim(matrix, index * length, length, 0)


def per_device(
    grad_out, route_weights, expert_ids, hot_pos, up_weight, down_weight, saved_inputs, saved_gates
):
    experts = lax.axis_size("grp") * lax.axis_size("j")
    device = lax.axis_index("grp") * lax.axis_size("j") + lax.axis_index("j")
    features = grad_out.shape[-1]
    hidden_units = saved_gates.shape[-1]
    token_count = grad_out.shape[2]
    slot_count = saved_inputs.shape[4]
    quarter_rows = slot_count // (REPL + 1)
    most_rows = REPL * quarter_rows
    hot_table = hot_pos[0]
    group_id = device // REPL
    local_pos = device % REPL
    owner_pos = jnp.sum(
        jnp.where(jnp.arange(hot_table.shape[0], dtype=jnp.int32) == group_id, hot_table, 0)
    )
    is_owner = local_pos == owner_pos
    own_up = up_weight[0, 0]
    own_down = down_weight[0, 0]
    owner_mask = is_owner.astype(jnp.bfloat16)
    hot_up, hot_down = lax.psum((own_up * owner_mask, own_down * owner_mask), "j")
    outputs = []
    token_grads = []
    for batch_idx in range(MB):
        expert_row = expert_ids[0, batch_idx].reshape(-1)
        token_flat_index = route_slots(
            expert_row, device, hot_table, experts, most_rows, slot_count
        )
        scaled = (
            route_weights[0, batch_idx][:, :, None]
            * grad_out[0, batch_idx][:, None, :].astype(jnp.float32)
        ).astype(jnp.bfloat16)
        routed_rows = scaled.reshape(-1, features)
        buffer = (
            jnp.zeros((experts * slot_count, features), jnp.bfloat16)
            .at[token_flat_index]
            .set(routed_rows)
            .reshape(experts, slot_count, features)
        )
        received = lax.all_to_all(buffer, EXPERT, split_axis=0, concat_axis=0, tiled=True)
        inputs_batch = saved_inputs[0, batch_idx, 0]
        gates_batch = saved_gates[0, batch_idx, 0]
        first_part = expert_rows(
            received[:, :most_rows],
            inputs_batch[:, :most_rows],
            gates_batch[:, :most_rows],
            own_up,
            own_down,
        )
        expert_second = expert_rows(
            received[:, most_rows:],
            inputs_batch[:, most_rows:],
            gates_batch[:, most_rows:],
            hot_up,
            hot_down,
        )
        back = jnp.concatenate([first_part[0], expert_second[0]], 1)
        gate_grad = jnp.concatenate([first_part[1], expert_second[1]], 1)
        outputs.append(
            (None, gate_grad, first_part[2], first_part[3], expert_second[2], expert_second[3])
        )
        returned = lax.all_to_all(back, EXPERT, split_axis=0, concat_axis=0, tiled=True)
        gathered = returned.reshape(experts * slot_count, features)[token_flat_index]
        summed = jnp.sum(gathered.reshape(token_count, TOP, features).astype(jnp.float32), axis=1)
        token_grad = (summed + grad_out[0, batch_idx].astype(jnp.float32)).astype(jnp.bfloat16)
        token_grads.append(from_behind(token_grad, "pipe", -1))
    own_up_sum = jnp.zeros((features, hidden_units), jnp.float32)
    own_down_sum = jnp.zeros((hidden_units, features), jnp.float32)
    rep_up_sum = jnp.zeros((features, hidden_units), jnp.float32)
    rep_down_sum = jnp.zeros((hidden_units, features), jnp.float32)
    for member in outputs:
        own_up_sum = own_up_sum + member[2]
        own_down_sum = own_down_sum + member[3]
        rep_up_sum = rep_up_sum + member[4]
        rep_down_sum = rep_down_sum + member[5]
    sent_back = jnp.stack(token_grads, 0)
    hot_up_part, hot_down_part = group_reduce_scatter(
        (rep_up_sum.astype(jnp.bfloat16), rep_down_sum.astype(jnp.bfloat16)), local_pos
    )
    hot_up_part = hot_up_part.astype(jnp.bfloat16)
    hot_down_part = hot_down_part.astype(jnp.bfloat16)
    up_grad = own_up_sum.astype(jnp.bfloat16)
    down_grad = own_down_sum.astype(jnp.bfloat16)
    gate_grads = jnp.stack([member[1] for member in outputs], 0)
    return (
        sent_back[None],
        up_grad[None, None],
        down_grad[None, None],
        gate_grads[None, :, None],
        hot_up_part[None, None],
        hot_down_part[None, None],
    )


EXPERT = ("grp", "j")


def solution(mesh):
    groups = mesh.devices.reshape(mesh.shape["pipe"], -1, REPL)
    group_mesh = jax.sharding.Mesh(groups, ("pipe", "grp", "j"))
    return jax.shard_map(
        per_device,
        mesh=group_mesh,
        in_specs=(
            P("pipe", None, EXPERT, None),
            P("pipe", None, EXPERT, None),
            P("pipe", None, EXPERT, None),
            P("pipe", None),
            P("pipe", EXPERT, None, None),
            P("pipe", EXPERT, None, None),
            P("pipe", None, EXPERT, None, None, None),
            P("pipe", None, EXPERT, None, None, None),
        ),
        out_specs=(
            P("pipe", None, EXPERT, None),
            P("pipe", EXPERT, None, None),
            P("pipe", EXPERT, None, None),
            P("pipe", None, EXPERT, None, None, None),
            P("pipe", EXPERT, None, None),
            P("pipe", EXPERT, None, None),
        ),
        check_vma=False,
    )
```

```python
import jax
import jax.numpy as jnp
from jax import lax
from jax.sharding import PartitionSpec as P

TOP = 8
REPL = 4
MB = 2


def partner(value, axis, bit):
    mask = 2**bit
    pairs = [(source, source ^ mask) for source in range(lax.axis_size(axis))]
    return lax.ppermute(value, axis, pairs)


def from_behind(block, axis, distance):
    devices = range(lax.axis_size(axis))
    route = [((i - distance) % len(devices), i) for i in devices]
    return lax.ppermute(block, axis, route)


def shift(value, distance):
    count = lax.axis_size("j")
    return lax.ppermute(value, "j", [(k, (k + distance) % count) for k in range(count)])


def quarter(matrix, index, pieces=REPL):
    length = matrix.shape[0] // pieces
    return lax.dynamic_slice_in_dim(matrix, index * length, length, 0)


def group_reduce_scatter(terms, local_pos):
    def parts(offset):
        return [quarter(t, (local_pos + offset) % REPL) for t in terms]

    def half(matrix, which):
        length = matrix.shape[0] // 2
        return matrix[which * length:(which + 1) * length]

    right_next, right_far = parts(1), parts(2)
    left_next = parts(3)
    to_right = [jnp.concatenate([a, half(b, 0)], 0) for a, b in zip(right_next, right_far)]
    to_left = [jnp.concatenate([a, half(b, 1)], 0) for a, b in zip(left_next, right_far)]
    from_left = shift(to_right, 1)
    from_right = shift(to_left, -1)
    sizes = [t.shape[0] // REPL for t in terms]
    relay_right = [m[n:] for m, n in zip(from_left, sizes)]
    relay_left = [m[n:] for m, n in zip(from_right, sizes)]
    far_first = shift(relay_right, 1)
    far_second = shift(relay_left, -1)
    mine = parts(0)
    sums = []
    for k, n in enumerate(sizes):
        total = (
            mine[k].astype(jnp.float32)
            + from_left[k][:n].astype(jnp.float32)
            + from_right[k][:n].astype(jnp.float32)
            + jnp.concatenate([far_first[k], far_second[k]], 0).astype(jnp.float32)
        )
        sums.append(total)
    return sums


def route_slots(expert_row, sender, hot_table, num_experts, most_rows, slot_count):
    onehot = (expert_row[:, None] == jnp.arange(num_experts, dtype=jnp.int32)[None, :]).astype(
        jnp.int32
    )
    order_pos = jnp.sum(jnp.cumsum(onehot, axis=0) * onehot, axis=1) - 1
    group_id = expert_row // REPL
    hot_count = hot_table.shape[0]
    owner_pos = jnp.sum(
        (group_id[:, None] == jnp.arange(hot_count, dtype=jnp.int32)[None, :]).astype(jnp.int32)
        * hot_table[None, :],
        axis=1,
    )
    is_hot = expert_row % REPL == owner_pos
    target = jnp.where(is_hot, REPL * group_id + (sender + order_pos) % REPL, expert_row)
    slot_pos = jnp.where(is_hot, most_rows + order_pos // REPL, order_pos)
    return target * slot_count + slot_pos


def expert_rows(grad_rows, input_rows, gate_rows, up_w, down_w):
    up_value = jnp.einsum("isd,df->isf", input_rows, up_w, preferred_element_type=jnp.float32)
    gate_value = gate_rows.astype(jnp.float32)
    gate_sig = jax.nn.sigmoid(gate_value)
    active = gate_value * gate_sig
    hidden = (active * up_value).astype(jnp.bfloat16)
    grad_hidden = jnp.einsum("isd,fd->isf", grad_rows, down_w, preferred_element_type=jnp.float32)
    grad_up = (grad_hidden * active).astype(jnp.bfloat16)
    grad_gate = (grad_hidden * up_value * gate_sig * (1.0 + gate_value * (1.0 - gate_sig))).astype(
        jnp.bfloat16
    )
    back_rows = jnp.einsum("isf,df->isd", grad_up, up_w, preferred_element_type=jnp.float32).astype(
        jnp.bfloat16
    )
    down_term = jnp.einsum("isf,isd->fd", hidden, grad_rows, preferred_element_type=jnp.float32)
    up_term = jnp.einsum("isd,isf->df", input_rows, grad_up, preferred_element_type=jnp.float32)
    return (back_rows, grad_gate, up_term, down_term)


def take_part(matrix, index, parts):
    length = matrix.shape[0] // parts
    return lax.dynamic_slice_in_dim(matrix, index * length, length, 0)


def per_device(
    grad_out, route_weights, expert_ids, hot_pos, up_weight, down_weight, saved_inputs, saved_gates
):
    experts = lax.axis_size("grp") * lax.axis_size("j")
    device = lax.axis_index("grp") * lax.axis_size("j") + lax.axis_index("j")
    features = grad_out.shape[-1]
    hidden_units = saved_gates.shape[-1]
    token_count = grad_out.shape[2]
    slot_count = saved_inputs.shape[4]
    quarter_rows = slot_count // (REPL + 1)
    most_rows = REPL * quarter_rows
    hot_table = hot_pos[0]
    group_id = device // REPL
    local_pos = device % REPL
    owner_pos = jnp.sum(
        jnp.where(jnp.arange(hot_table.shape[0], dtype=jnp.int32) == group_id, hot_table, 0)
    )
    is_owner = local_pos == owner_pos
    own_up = up_weight[0, 0]
    own_down = down_weight[0, 0]
    owner_mask = is_owner.astype(jnp.bfloat16)
    hot_up, hot_down = lax.psum((own_up * owner_mask, own_down * owner_mask), "j")
    outputs = []
    token_grads = []
    flat_index = []
    routed = []
    for batch_idx in range(MB):
        expert_row = expert_ids[0, batch_idx].reshape(-1)
        slot_index = route_slots(expert_row, device, hot_table, experts, most_rows, slot_count)
        target = slot_index // slot_count
        flat_index.append(slot_index + (target * (MB - 1) + batch_idx) * slot_count)
        scaled = (
            route_weights[0, batch_idx][:, :, None]
            * grad_out[0, batch_idx][:, None, :].astype(jnp.float32)
        ).astype(jnp.bfloat16)
        routed.append(scaled.reshape(-1, features))
    flat_index = jnp.concatenate(flat_index, 0)
    buffer = (
        jnp.zeros((experts * MB * slot_count, features), jnp.bfloat16)
        .at[flat_index]
        .set(jnp.concatenate(routed, 0))
        .reshape(experts, MB, slot_count, features)
    )
    received_all = lax.all_to_all(buffer, EXPERT, split_axis=0, concat_axis=0, tiled=True)
    backs = []
    for batch_idx in range(MB):
        received = received_all[:, batch_idx]
        inputs_batch = saved_inputs[0, batch_idx, 0]
        gates_batch = saved_gates[0, batch_idx, 0]
        first_part = expert_rows(
            received[:, :most_rows],
            inputs_batch[:, :most_rows],
            gates_batch[:, :most_rows],
            own_up,
            own_down,
        )
        expert_second = expert_rows(
            received[:, most_rows:],
            inputs_batch[:, most_rows:],
            gates_batch[:, most_rows:],
            hot_up,
            hot_down,
        )
        backs.append(jnp.concatenate([first_part[0], expert_second[0]], 1))
        gate_grad = jnp.concatenate([first_part[1], expert_second[1]], 1)
        outputs.append(
            (None, gate_grad, first_part[2], first_part[3], expert_second[2], expert_second[3])
        )
    returned = lax.all_to_all(jnp.stack(backs, 1), EXPERT, split_axis=0, concat_axis=0, tiled=True)
    gathered = returned.reshape(experts * MB * slot_count, features)[flat_index]
    summed = jnp.sum(gathered.reshape(MB, token_count, TOP, features).astype(jnp.float32), axis=2)
    token_grads = (summed + grad_out[0].astype(jnp.float32)).astype(jnp.bfloat16)
    own_up_sum = jnp.zeros((features, hidden_units), jnp.float32)
    own_down_sum = jnp.zeros((hidden_units, features), jnp.float32)
    rep_up_sum = jnp.zeros((features, hidden_units), jnp.float32)
    rep_down_sum = jnp.zeros((hidden_units, features), jnp.float32)
    for member in outputs:
        own_up_sum = own_up_sum + member[2]
        own_down_sum = own_down_sum + member[3]
        rep_up_sum = rep_up_sum + member[4]
        rep_down_sum = rep_down_sum + member[5]
    sent_back = from_behind(token_grads, "pipe", -1)
    hot_up_part, hot_down_part = group_reduce_scatter(
        (rep_up_sum.astype(jnp.bfloat16), rep_down_sum.astype(jnp.bfloat16)), local_pos
    )
    hot_up_part = hot_up_part.astype(jnp.bfloat16)
    hot_down_part = hot_down_part.astype(jnp.bfloat16)
    up_grad = own_up_sum.astype(jnp.bfloat16)
    down_grad = own_down_sum.astype(jnp.bfloat16)
    gate_grads = jnp.stack([member[1] for member in outputs], 0)
    return (
        sent_back[None],
        up_grad[None, None],
        down_grad[None, None],
        gate_grads[None, :, None],
        hot_up_part[None, None],
        hot_down_part[None, None],
    )


EXPERT = ("grp", "j")


def solution(mesh):
    groups = mesh.devices.reshape(mesh.shape["pipe"], -1, REPL)
    group_mesh = jax.sharding.Mesh(groups, ("pipe", "grp", "j"))
    return jax.shard_map(
        per_device,
        mesh=group_mesh,
        in_specs=(
            P("pipe", None, EXPERT, None),
            P("pipe", None, EXPERT, None),
            P("pipe", None, EXPERT, None),
            P("pipe", None),
            P("pipe", EXPERT, None, None),
            P("pipe", EXPERT, None, None),
            P("pipe", None, EXPERT, None, None, None),
            P("pipe", None, EXPERT, None, None, None),
        ),
        out_specs=(
            P("pipe", None, EXPERT, None),
            P("pipe", EXPERT, None, None),
            P("pipe", EXPERT, None, None),
            P("pipe", None, EXPERT, None, None, None),
            P("pipe", EXPERT, None, None),
            P("pipe", EXPERT, None, None),
        ),
        check_vma=False,
    )
```

```python
import jax
import jax.numpy as jnp
from jax import lax
from jax.sharding import PartitionSpec as P

TOP = 8
REPL = 4
MB = 2


def partner(value, axis, bit):
    mask = 2**bit
    pairs = [(source, source ^ mask) for source in range(lax.axis_size(axis))]
    return lax.ppermute(value, axis, pairs)


def from_behind(block, axis, distance):
    devices = range(lax.axis_size(axis))
    route = [((i - distance) % len(devices), i) for i in devices]
    return lax.ppermute(block, axis, route)


def shift(value, distance):
    count = lax.axis_size("j")
    return lax.ppermute(value, "j", [(k, (k + distance) % count) for k in range(count)])


def quarter(matrix, index, pieces=REPL):
    length = matrix.shape[0] // pieces
    return lax.dynamic_slice_in_dim(matrix, index * length, length, 0)


def group_reduce_scatter(terms, local_pos):
    def parts(offset):
        return [quarter(t, (local_pos + offset) % REPL) for t in terms]

    def half(matrix, which):
        length = matrix.shape[0] // 2
        return matrix[which * length:(which + 1) * length]

    right_next, right_far = parts(1), parts(2)
    left_next = parts(3)
    to_right = [jnp.concatenate([a, half(b, 0)], 0) for a, b in zip(right_next, right_far)]
    to_left = [jnp.concatenate([a, half(b, 1)], 0) for a, b in zip(left_next, right_far)]
    from_left = shift(to_right, 1)
    from_right = shift(to_left, -1)
    sizes = [t.shape[0] // REPL for t in terms]
    relay_right = [m[n:] for m, n in zip(from_left, sizes)]
    relay_left = [m[n:] for m, n in zip(from_right, sizes)]
    far_first = shift(relay_right, 1)
    far_second = shift(relay_left, -1)
    mine = parts(0)
    sums = []
    for k, n in enumerate(sizes):
        total = (
            mine[k].astype(jnp.float32)
            + from_left[k][:n].astype(jnp.float32)
            + from_right[k][:n].astype(jnp.float32)
            + jnp.concatenate([far_first[k], far_second[k]], 0).astype(jnp.float32)
        )
        sums.append(total)
    return sums


def route_slots(expert_row, sender, hot_table, num_experts, most_rows, slot_count):
    onehot = (expert_row[:, None] == jnp.arange(num_experts, dtype=jnp.int32)[None, :]).astype(
        jnp.int32
    )
    order_pos = jnp.sum(jnp.cumsum(onehot, axis=0) * onehot, axis=1) - 1
    group_id = expert_row // REPL
    hot_count = hot_table.shape[0]
    owner_pos = jnp.sum(
        (group_id[:, None] == jnp.arange(hot_count, dtype=jnp.int32)[None, :]).astype(jnp.int32)
        * hot_table[None, :],
        axis=1,
    )
    is_hot = expert_row % REPL == owner_pos
    target = jnp.where(is_hot, REPL * group_id + (sender + order_pos) % REPL, expert_row)
    slot_pos = jnp.where(is_hot, most_rows + order_pos // REPL, order_pos)
    return target * slot_count + slot_pos


def expert_rows(grad_rows, input_rows, gate_rows, up_w, down_w):
    up_value = jnp.einsum("isd,df->isf", input_rows, up_w, preferred_element_type=jnp.float32)
    gate_value = gate_rows.astype(jnp.float32)
    gate_sig = jax.nn.sigmoid(gate_value)
    active = gate_value * gate_sig
    hidden = (active * up_value).astype(jnp.bfloat16)
    grad_hidden = jnp.einsum("isd,fd->isf", grad_rows, down_w, preferred_element_type=jnp.float32)
    grad_up = (grad_hidden * active).astype(jnp.bfloat16)
    grad_gate = (grad_hidden * up_value * gate_sig * (1.0 + gate_value * (1.0 - gate_sig))).astype(
        jnp.bfloat16
    )
    back_rows = jnp.einsum("isf,df->isd", grad_up, up_w, preferred_element_type=jnp.float32).astype(
        jnp.bfloat16
    )
    down_term = jnp.einsum("isf,isd->fd", hidden, grad_rows, preferred_element_type=jnp.float32)
    up_term = jnp.einsum("isd,isf->df", input_rows, grad_up, preferred_element_type=jnp.float32)
    return (back_rows, grad_gate, up_term, down_term)


def take_part(matrix, index, parts):
    length = matrix.shape[0] // parts
    return lax.dynamic_slice_in_dim(matrix, index * length, length, 0)


def per_device(
    grad_out, route_weights, expert_ids, hot_pos, up_weight, down_weight, saved_inputs, saved_gates
):
    experts = lax.axis_size("grp") * lax.axis_size("j")
    device = lax.axis_index("grp") * lax.axis_size("j") + lax.axis_index("j")
    features = grad_out.shape[-1]
    hidden_units = saved_gates.shape[-1]
    token_count = grad_out.shape[2]
    slot_count = saved_inputs.shape[4]
    quarter_rows = slot_count // (REPL + 1)
    most_rows = REPL * quarter_rows
    hot_table = hot_pos[0]
    group_id = device // REPL
    local_pos = device % REPL
    owner_pos = jnp.sum(
        jnp.where(jnp.arange(hot_table.shape[0], dtype=jnp.int32) == group_id, hot_table, 0)
    )
    is_owner = local_pos == owner_pos
    own_up = up_weight[0, 0]
    own_down = down_weight[0, 0]
    owner_mask = is_owner.astype(jnp.bfloat16)
    hot_up, hot_down = lax.psum((own_up * owner_mask, own_down * owner_mask), "j")
    outputs = []
    token_grads = []
    flat_index = []
    back_index = []
    routed = []
    for batch_idx in range(MB):
        expert_row = expert_ids[0, batch_idx].reshape(-1)
        slot_index = route_slots(expert_row, device, hot_table, experts, most_rows, slot_count)
        target = slot_index // slot_count
        flat_index.append(slot_index + (target * (MB - 1) + batch_idx) * slot_count)
        slot_pos = slot_index % slot_count
        quarter_rows = slot_count - most_rows
        back_index.append(
            jnp.where(
                slot_pos < most_rows,
                (target * MB + batch_idx) * most_rows + slot_pos,
                experts * MB * most_rows
                + (target * MB + batch_idx) * quarter_rows
                + slot_pos
                - most_rows,
            )
        )
        scaled = (
            route_weights[0, batch_idx][:, :, None]
            * grad_out[0, batch_idx][:, None, :].astype(jnp.float32)
        ).astype(jnp.bfloat16)
        routed.append(scaled.reshape(-1, features))
    flat_index = jnp.concatenate(flat_index, 0)
    back_index = jnp.concatenate(back_index, 0)
    buffer = (
        jnp.zeros((experts * MB * slot_count, features), jnp.bfloat16)
        .at[flat_index]
        .set(jnp.concatenate(routed, 0))
        .reshape(experts, MB, slot_count, features)
    )
    received_all = lax.all_to_all(buffer, EXPERT, split_axis=0, concat_axis=0, tiled=True)
    backs = []
    for batch_idx in range(MB):
        received = received_all[:, batch_idx]
        inputs_batch = saved_inputs[0, batch_idx, 0]
        gates_batch = saved_gates[0, batch_idx, 0]
        first_part = expert_rows(
            received[:, :most_rows],
            inputs_batch[:, :most_rows],
            gates_batch[:, :most_rows],
            own_up,
            own_down,
        )
        expert_second = expert_rows(
            received[:, most_rows:],
            inputs_batch[:, most_rows:],
            gates_batch[:, most_rows:],
            hot_up,
            hot_down,
        )
        backs.append((first_part[0], expert_second[0]))
        gate_grad = jnp.concatenate([first_part[1], expert_second[1]], 1)
        outputs.append(
            (None, gate_grad, first_part[2], first_part[3], expert_second[2], expert_second[3])
        )
    returned_own = lax.all_to_all(
        jnp.stack([part[0] for part in backs], 1), EXPERT, split_axis=0, concat_axis=0, tiled=True
    )
    returned_hot = lax.all_to_all(
        jnp.stack([part[1] for part in backs], 1), EXPERT, split_axis=0, concat_axis=0, tiled=True
    )
    returned = jnp.concatenate(
        [returned_own.reshape(-1, features), returned_hot.reshape(-1, features)], 0
    )
    gathered = returned[back_index]
    summed = jnp.sum(gathered.reshape(MB, token_count, TOP, features).astype(jnp.float32), axis=2)
    token_grads = (summed + grad_out[0].astype(jnp.float32)).astype(jnp.bfloat16)
    own_up_sum = jnp.zeros((features, hidden_units), jnp.float32)
    own_down_sum = jnp.zeros((hidden_units, features), jnp.float32)
    rep_up_sum = jnp.zeros((features, hidden_units), jnp.float32)
    rep_down_sum = jnp.zeros((hidden_units, features), jnp.float32)
    for member in outputs:
        own_up_sum = own_up_sum + member[2]
        own_down_sum = own_down_sum + member[3]
        rep_up_sum = rep_up_sum + member[4]
        rep_down_sum = rep_down_sum + member[5]
    sent_back = from_behind(token_grads, "pipe", -1)
    hot_up_part, hot_down_part = group_reduce_scatter(
        (rep_up_sum.astype(jnp.bfloat16), rep_down_sum.astype(jnp.bfloat16)), local_pos
    )
    hot_up_part = hot_up_part.astype(jnp.bfloat16)
    hot_down_part = hot_down_part.astype(jnp.bfloat16)
    up_grad = own_up_sum.astype(jnp.bfloat16)
    down_grad = own_down_sum.astype(jnp.bfloat16)
    gate_grads = jnp.stack([member[1] for member in outputs], 0)
    return (
        sent_back[None],
        up_grad[None, None],
        down_grad[None, None],
        gate_grads[None, :, None],
        hot_up_part[None, None],
        hot_down_part[None, None],
    )


EXPERT = ("grp", "j")


def solution(mesh):
    groups = mesh.devices.reshape(mesh.shape["pipe"], -1, REPL)
    group_mesh = jax.sharding.Mesh(groups, ("pipe", "grp", "j"))
    return jax.shard_map(
        per_device,
        mesh=group_mesh,
        in_specs=(
            P("pipe", None, EXPERT, None),
            P("pipe", None, EXPERT, None),
            P("pipe", None, EXPERT, None),
            P("pipe", None),
            P("pipe", EXPERT, None, None),
            P("pipe", EXPERT, None, None),
            P("pipe", None, EXPERT, None, None, None),
            P("pipe", None, EXPERT, None, None, None),
        ),
        out_specs=(
            P("pipe", None, EXPERT, None),
            P("pipe", EXPERT, None, None),
            P("pipe", EXPERT, None, None),
            P("pipe", None, EXPERT, None, None, None),
            P("pipe", EXPERT, None, None),
            P("pipe", EXPERT, None, None),
        ),
        check_vma=False,
    )
```

```python
import jax
import numpy as np
import jax.numpy as jnp
from jax import lax
from jax.sharding import PartitionSpec as P

TOP = 8
REPL = 4
MB = 2


def partner(value, axis, bit):
    mask = 2**bit
    pairs = [(source, source ^ mask) for source in range(lax.axis_size(axis))]
    return lax.ppermute(value, axis, pairs)


def from_behind(block, axis, distance):
    devices = range(lax.axis_size(axis))
    route = [((i - distance) % len(devices), i) for i in devices]
    return lax.ppermute(block, axis, route)


def shift(value, distance):
    count = lax.axis_size("j")
    return lax.ppermute(value, "j", [(k, (k + distance) % count) for k in range(count)])


def quarter(matrix, index, pieces=REPL):
    length = matrix.shape[0] // pieces
    return lax.dynamic_slice_in_dim(matrix, index * length, length, 0)


def group_reduce_scatter(terms, local_pos):
    def parts(offset):
        return [quarter(t, (local_pos + offset) % REPL) for t in terms]

    def half(matrix, which):
        length = matrix.shape[0] // 2
        return matrix[which * length:(which + 1) * length]

    right_next, right_far = parts(1), parts(2)
    left_next = parts(3)
    to_right = [jnp.concatenate([a, half(b, 0)], 0) for a, b in zip(right_next, right_far)]
    to_left = [jnp.concatenate([a, half(b, 1)], 0) for a, b in zip(left_next, right_far)]
    from_left = shift(to_right, 1)
    from_right = shift(to_left, -1)
    sizes = [t.shape[0] // REPL for t in terms]
    relay_right = [m[n:] for m, n in zip(from_left, sizes)]
    relay_left = [m[n:] for m, n in zip(from_right, sizes)]
    far_first = shift(relay_right, 1)
    far_second = shift(relay_left, -1)
    mine = parts(0)
    sums = []
    for k, n in enumerate(sizes):
        total = (
            mine[k].astype(jnp.float32)
            + from_left[k][:n].astype(jnp.float32)
            + from_right[k][:n].astype(jnp.float32)
            + jnp.concatenate([far_first[k], far_second[k]], 0).astype(jnp.float32)
        )
        sums.append(total)
    return sums


def route_slots(expert_row, sender, hot_table, num_experts, most_rows, slot_count):
    onehot = (expert_row[:, None] == jnp.arange(num_experts, dtype=jnp.int32)[None, :]).astype(
        jnp.int32
    )
    order_pos = jnp.sum(jnp.cumsum(onehot, axis=0) * onehot, axis=1) - 1
    group_id = expert_row // REPL
    hot_count = hot_table.shape[0]
    owner_pos = jnp.sum(
        (group_id[:, None] == jnp.arange(hot_count, dtype=jnp.int32)[None, :]).astype(jnp.int32)
        * hot_table[None, :],
        axis=1,
    )
    is_hot = expert_row % REPL == owner_pos
    target = jnp.where(is_hot, REPL * group_id + (sender + order_pos) % REPL, expert_row)
    slot_pos = jnp.where(is_hot, most_rows + order_pos // REPL, order_pos)
    return target * slot_count + slot_pos


def expert_rows(grad_rows, input_rows, gate_rows, up_w, down_w):
    up_value = jnp.einsum("isd,df->isf", input_rows, up_w, preferred_element_type=jnp.float32)
    gate_value = gate_rows.astype(jnp.float32)
    gate_sig = jax.nn.sigmoid(gate_value)
    active = gate_value * gate_sig
    hidden = (active * up_value).astype(jnp.bfloat16)
    grad_hidden = jnp.einsum("isd,fd->isf", grad_rows, down_w, preferred_element_type=jnp.float32)
    grad_up = (grad_hidden * active).astype(jnp.bfloat16)
    grad_gate = (grad_hidden * up_value * gate_sig * (1.0 + gate_value * (1.0 - gate_sig))).astype(
        jnp.bfloat16
    )
    back_rows = jnp.einsum("isf,df->isd", grad_up, up_w, preferred_element_type=jnp.float32).astype(
        jnp.bfloat16
    )
    down_term = jnp.einsum("isf,isd->fd", hidden, grad_rows, preferred_element_type=jnp.float32)
    up_term = jnp.einsum("isd,isf->df", input_rows, grad_up, preferred_element_type=jnp.float32)
    return (back_rows, grad_gate, up_term, down_term)


def take_part(matrix, index, parts):
    length = matrix.shape[0] // parts
    return lax.dynamic_slice_in_dim(matrix, index * length, length, 0)


def per_device(
    grad_out, route_weights, expert_ids, hot_pos, up_weight, down_weight, saved_inputs, saved_gates
):
    experts = lax.axis_size("grp") * lax.axis_size("j")
    device = lax.axis_index("grp") * lax.axis_size("j") + lax.axis_index("j")
    features = grad_out.shape[-1]
    hidden_units = saved_gates.shape[-1]
    token_count = grad_out.shape[2]
    slot_count = saved_inputs.shape[4]
    quarter_rows = slot_count // (REPL + 1)
    most_rows = REPL * quarter_rows
    hot_table = hot_pos[0]
    group_id = device // REPL
    local_pos = device % REPL
    owner_pos = jnp.sum(
        jnp.where(jnp.arange(hot_table.shape[0], dtype=jnp.int32) == group_id, hot_table, 0)
    )
    is_owner = local_pos == owner_pos
    own_up = up_weight[0, 0]
    own_down = down_weight[0, 0]
    owner_mask = is_owner.astype(jnp.bfloat16)
    hot_up, hot_down = lax.psum((own_up * owner_mask, own_down * owner_mask), "j")
    outputs = []
    token_grads = []
    flat_index = []
    back_index = []
    routed = []
    for batch_idx in range(MB):
        expert_row = expert_ids[0, batch_idx].reshape(-1)
        slot_index = route_slots(expert_row, device, hot_table, experts, most_rows, slot_count)
        target = slot_index // slot_count
        flat_index.append(slot_index + (target * (MB - 1) + batch_idx) * slot_count)
        slot_pos = slot_index % slot_count
        quarter_rows = slot_count - most_rows
        back_index.append(
            jnp.where(
                slot_pos < most_rows,
                (target * MB + batch_idx) * most_rows + slot_pos,
                experts * MB * most_rows
                + (target * MB + batch_idx) * quarter_rows
                + slot_pos
                - most_rows,
            )
        )
        scaled = (
            route_weights[0, batch_idx][:, :, None]
            * grad_out[0, batch_idx][:, None, :].astype(jnp.float32)
        ).astype(jnp.bfloat16)
        routed.append(scaled.reshape(-1, features))
    flat_index = jnp.concatenate(flat_index, 0)
    back_index = jnp.concatenate(back_index, 0)
    targets = flat_index // (MB * slot_count)
    slots = flat_index % slot_count
    batches = np.repeat(np.arange(MB), token_count * TOP)
    place = (
        (jnp.arange(experts)[:, None, None, None] == targets)
        & (np.arange(MB)[None, :, None, None] == batches)
        & (jnp.arange(slot_count)[None, None, :, None] == slots)
    ).astype(jnp.bfloat16)
    buffer = jnp.einsum(
        "qbcr,rf->qbcf", place, jnp.concatenate(routed, 0), preferred_element_type=jnp.float32
    ).astype(jnp.bfloat16)
    received_all = lax.all_to_all(buffer, EXPERT, split_axis=0, concat_axis=0, tiled=True)
    backs = []
    for batch_idx in range(MB):
        received = received_all[:, batch_idx]
        inputs_batch = saved_inputs[0, batch_idx, 0]
        gates_batch = saved_gates[0, batch_idx, 0]
        first_part = expert_rows(
            received[:, :most_rows],
            inputs_batch[:, :most_rows],
            gates_batch[:, :most_rows],
            own_up,
            own_down,
        )
        expert_second = expert_rows(
            received[:, most_rows:],
            inputs_batch[:, most_rows:],
            gates_batch[:, most_rows:],
            hot_up,
            hot_down,
        )
        backs.append((first_part[0], expert_second[0]))
        gate_grad = jnp.concatenate([first_part[1], expert_second[1]], 1)
        outputs.append(
            (None, gate_grad, first_part[2], first_part[3], expert_second[2], expert_second[3])
        )
    returned_own = lax.all_to_all(
        jnp.stack([part[0] for part in backs], 1), EXPERT, split_axis=0, concat_axis=0, tiled=True
    )
    returned_hot = lax.all_to_all(
        jnp.stack([part[1] for part in backs], 1), EXPERT, split_axis=0, concat_axis=0, tiled=True
    )
    returned = jnp.concatenate(
        [returned_own.reshape(-1, features), returned_hot.reshape(-1, features)], 0
    )
    gathered = returned[back_index]
    summed = jnp.sum(gathered.reshape(MB, token_count, TOP, features).astype(jnp.float32), axis=2)
    token_grads = (summed + grad_out[0].astype(jnp.float32)).astype(jnp.bfloat16)
    own_up_sum = jnp.zeros((features, hidden_units), jnp.float32)
    own_down_sum = jnp.zeros((hidden_units, features), jnp.float32)
    rep_up_sum = jnp.zeros((features, hidden_units), jnp.float32)
    rep_down_sum = jnp.zeros((hidden_units, features), jnp.float32)
    for member in outputs:
        own_up_sum = own_up_sum + member[2]
        own_down_sum = own_down_sum + member[3]
        rep_up_sum = rep_up_sum + member[4]
        rep_down_sum = rep_down_sum + member[5]
    sent_back = from_behind(token_grads, "pipe", -1)
    hot_up_part, hot_down_part = group_reduce_scatter(
        (rep_up_sum.astype(jnp.bfloat16), rep_down_sum.astype(jnp.bfloat16)), local_pos
    )
    hot_up_part = hot_up_part.astype(jnp.bfloat16)
    hot_down_part = hot_down_part.astype(jnp.bfloat16)
    up_grad = own_up_sum.astype(jnp.bfloat16)
    down_grad = own_down_sum.astype(jnp.bfloat16)
    gate_grads = jnp.stack([member[1] for member in outputs], 0)
    return (
        sent_back[None],
        up_grad[None, None],
        down_grad[None, None],
        gate_grads[None, :, None],
        hot_up_part[None, None],
        hot_down_part[None, None],
    )


EXPERT = ("grp", "j")


def solution(mesh):
    groups = mesh.devices.reshape(mesh.shape["pipe"], -1, REPL)
    group_mesh = jax.sharding.Mesh(groups, ("pipe", "grp", "j"))
    return jax.shard_map(
        per_device,
        mesh=group_mesh,
        in_specs=(
            P("pipe", None, EXPERT, None),
            P("pipe", None, EXPERT, None),
            P("pipe", None, EXPERT, None),
            P("pipe", None),
            P("pipe", EXPERT, None, None),
            P("pipe", EXPERT, None, None),
            P("pipe", None, EXPERT, None, None, None),
            P("pipe", None, EXPERT, None, None, None),
        ),
        out_specs=(
            P("pipe", None, EXPERT, None),
            P("pipe", EXPERT, None, None),
            P("pipe", EXPERT, None, None),
            P("pipe", None, EXPERT, None, None, None),
            P("pipe", EXPERT, None, None),
            P("pipe", EXPERT, None, None),
        ),
        check_vma=False,
    )
```

```python
import jax
import numpy as np
import jax.numpy as jnp
from jax import lax
from jax.sharding import PartitionSpec as P

TOP = 8
REPL = 4
MB = 2


def partner(value, axis, bit):
    mask = 2**bit
    pairs = [(source, source ^ mask) for source in range(lax.axis_size(axis))]
    return lax.ppermute(value, axis, pairs)


def from_behind(block, axis, distance):
    devices = range(lax.axis_size(axis))
    route = [((i - distance) % len(devices), i) for i in devices]
    return lax.ppermute(block, axis, route)


def shift(value, distance):
    count = lax.axis_size("j")
    return lax.ppermute(value, "j", [(k, (k + distance) % count) for k in range(count)])


def quarter(matrix, index, pieces=REPL):
    length = matrix.shape[0] // pieces
    return lax.dynamic_slice_in_dim(matrix, index * length, length, 0)


def group_reduce_scatter(terms, local_pos):
    def parts(offset):
        return [quarter(t, (local_pos + offset) % REPL) for t in terms]

    def half(matrix, which):
        length = matrix.shape[0] // 2
        return matrix[which * length:(which + 1) * length]

    right_next, right_far = parts(1), parts(2)
    left_next = parts(3)
    to_right = [jnp.concatenate([a, half(b, 0)], 0) for a, b in zip(right_next, right_far)]
    to_left = [jnp.concatenate([a, half(b, 1)], 0) for a, b in zip(left_next, right_far)]
    from_left = shift(to_right, 1)
    from_right = shift(to_left, -1)
    sizes = [t.shape[0] // REPL for t in terms]
    relay_right = [m[n:] for m, n in zip(from_left, sizes)]
    relay_left = [m[n:] for m, n in zip(from_right, sizes)]
    far_first = shift(relay_right, 1)
    far_second = shift(relay_left, -1)
    mine = parts(0)
    sums = []
    for k, n in enumerate(sizes):
        total = (
            mine[k].astype(jnp.float32)
            + from_left[k][:n].astype(jnp.float32)
            + from_right[k][:n].astype(jnp.float32)
            + jnp.concatenate([far_first[k], far_second[k]], 0).astype(jnp.float32)
        )
        sums.append(total)
    return sums


def route_slots(expert_row, sender, hot_table, num_experts, most_rows, slot_count):
    onehot = (expert_row[:, None] == jnp.arange(num_experts, dtype=jnp.int32)[None, :]).astype(
        jnp.int32
    )
    order_pos = jnp.sum(jnp.cumsum(onehot, axis=0) * onehot, axis=1) - 1
    group_id = expert_row // REPL
    hot_count = hot_table.shape[0]
    owner_pos = jnp.sum(
        (group_id[:, None] == jnp.arange(hot_count, dtype=jnp.int32)[None, :]).astype(jnp.int32)
        * hot_table[None, :],
        axis=1,
    )
    is_hot = expert_row % REPL == owner_pos
    target = jnp.where(is_hot, REPL * group_id + (sender + order_pos) % REPL, expert_row)
    slot_pos = jnp.where(is_hot, most_rows + order_pos // REPL, order_pos)
    return target * slot_count + slot_pos


def expert_rows(grad_rows, input_rows, gate_rows, up_w, down_w):
    up_value = jnp.einsum("isd,df->isf", input_rows, up_w, preferred_element_type=jnp.float32)
    gate_value = gate_rows.astype(jnp.float32)
    gate_sig = jax.nn.sigmoid(gate_value)
    active = gate_value * gate_sig
    hidden = (active * up_value).astype(jnp.bfloat16)
    grad_hidden = jnp.einsum("isd,fd->isf", grad_rows, down_w, preferred_element_type=jnp.float32)
    grad_up = (grad_hidden * active).astype(jnp.bfloat16)
    grad_gate = (grad_hidden * up_value * gate_sig * (1.0 + gate_value * (1.0 - gate_sig))).astype(
        jnp.bfloat16
    )
    back_rows = jnp.einsum("isf,df->isd", grad_up, up_w, preferred_element_type=jnp.float32).astype(
        jnp.bfloat16
    )
    down_term = jnp.einsum("isf,isd->fd", hidden, grad_rows, preferred_element_type=jnp.float32)
    up_term = jnp.einsum("isd,isf->df", input_rows, grad_up, preferred_element_type=jnp.float32)
    return (back_rows, grad_gate, up_term, down_term)


def take_part(matrix, index, parts):
    length = matrix.shape[0] // parts
    return lax.dynamic_slice_in_dim(matrix, index * length, length, 0)


def per_device(
    grad_out, route_weights, expert_ids, hot_pos, up_weight, down_weight, saved_inputs, saved_gates
):
    experts = lax.axis_size("grp") * lax.axis_size("j")
    device = lax.axis_index("grp") * lax.axis_size("j") + lax.axis_index("j")
    features = grad_out.shape[-1]
    hidden_units = saved_gates.shape[-1]
    token_count = grad_out.shape[2]
    slot_count = saved_inputs.shape[4]
    quarter_rows = slot_count // (REPL + 1)
    most_rows = REPL * quarter_rows
    hot_table = hot_pos[0]
    group_id = device // REPL
    local_pos = device % REPL
    owner_pos = jnp.sum(
        jnp.where(jnp.arange(hot_table.shape[0], dtype=jnp.int32) == group_id, hot_table, 0)
    )
    is_owner = local_pos == owner_pos
    own_up = up_weight[0, 0]
    own_down = down_weight[0, 0]
    owner_mask = is_owner.astype(jnp.bfloat16)
    hot_up, hot_down = lax.psum((own_up * owner_mask, own_down * owner_mask), "j")
    outputs = []
    token_grads = []
    flat_index = []
    back_index = []
    routed = []
    for batch_idx in range(MB):
        expert_row = expert_ids[0, batch_idx].reshape(-1)
        slot_index = route_slots(expert_row, device, hot_table, experts, most_rows, slot_count)
        target = slot_index // slot_count
        flat_index.append(slot_index + (target * (MB - 1) + batch_idx) * slot_count)
        slot_pos = slot_index % slot_count
        quarter_rows = slot_count - most_rows
        back_index.append(
            jnp.where(
                slot_pos < most_rows,
                (target * MB + batch_idx) * most_rows + slot_pos,
                experts * MB * most_rows
                + (target * MB + batch_idx) * quarter_rows
                + slot_pos
                - most_rows,
            )
        )
        scaled = (
            route_weights[0, batch_idx][:, :, None]
            * grad_out[0, batch_idx][:, None, :].astype(jnp.float32)
        ).astype(jnp.bfloat16)
        routed.append(scaled.reshape(-1, features))
    flat_index = jnp.concatenate(flat_index, 0)
    back_index = jnp.concatenate(back_index, 0)
    targets = flat_index // (MB * slot_count)
    slots = flat_index % slot_count
    batches = np.repeat(np.arange(MB), token_count * TOP)
    place = (
        (jnp.arange(experts)[:, None, None, None] == targets)
        & (np.arange(MB)[None, :, None, None] == batches)
        & (jnp.arange(slot_count)[None, None, :, None] == slots)
    ).astype(jnp.bfloat16)
    buffer = jnp.einsum(
        "qbcr,rf->qbcf", place, jnp.concatenate(routed, 0), preferred_element_type=jnp.float32
    ).astype(jnp.bfloat16)
    received_all = lax.all_to_all(buffer, EXPERT, split_axis=0, concat_axis=0, tiled=True)
    backs = []
    for batch_idx in range(MB):
        received = received_all[:, batch_idx]
        inputs_batch = saved_inputs[0, batch_idx, 0]
        gates_batch = saved_gates[0, batch_idx, 0]
        first_part = expert_rows(
            received[:, :most_rows],
            inputs_batch[:, :most_rows],
            gates_batch[:, :most_rows],
            own_up,
            own_down,
        )
        expert_second = expert_rows(
            received[:, most_rows:],
            inputs_batch[:, most_rows:],
            gates_batch[:, most_rows:],
            hot_up,
            hot_down,
        )
        backs.append((first_part[0], expert_second[0]))
        gate_grad = jnp.concatenate([first_part[1], expert_second[1]], 1)
        outputs.append(
            (None, gate_grad, first_part[2], first_part[3], expert_second[2], expert_second[3])
        )
    returned_own = lax.all_to_all(
        jnp.stack([part[0] for part in backs], 1), EXPERT, split_axis=0, concat_axis=0, tiled=True
    )
    returned_hot = lax.all_to_all(
        jnp.stack([part[1] for part in backs], 1), EXPERT, split_axis=0, concat_axis=0, tiled=True
    )
    token_targets = targets.reshape(MB * token_count, TOP)
    token_slots = slots.reshape(MB * token_count, TOP)
    token_batch = np.arange(MB)[None, :] == np.repeat(np.arange(MB), token_count)[:, None]
    by_target = (token_targets[:, :, None] == jnp.arange(experts)).astype(jnp.bfloat16)

    def pick(slot_range):
        by_slot = (token_slots[:, :, None] == slot_range).astype(jnp.bfloat16)
        picks = jnp.einsum("ukq,ukc->uqc", by_target, by_slot)
        return picks[:, :, None, :] * token_batch[:, None, :, None].astype(jnp.bfloat16)

    summed = jnp.einsum(
        "uqbc,qbcf->uf", pick(jnp.arange(most_rows)), returned_own,
        preferred_element_type=jnp.float32,
    ) + jnp.einsum(
        "uqbc,qbcf->uf", pick(jnp.arange(most_rows, slot_count)), returned_hot,
        preferred_element_type=jnp.float32,
    )
    summed = summed.reshape(MB, token_count, features)
    token_grads = (summed + grad_out[0].astype(jnp.float32)).astype(jnp.bfloat16)
    own_up_sum = jnp.zeros((features, hidden_units), jnp.float32)
    own_down_sum = jnp.zeros((hidden_units, features), jnp.float32)
    rep_up_sum = jnp.zeros((features, hidden_units), jnp.float32)
    rep_down_sum = jnp.zeros((hidden_units, features), jnp.float32)
    for member in outputs:
        own_up_sum = own_up_sum + member[2]
        own_down_sum = own_down_sum + member[3]
        rep_up_sum = rep_up_sum + member[4]
        rep_down_sum = rep_down_sum + member[5]
    sent_back = from_behind(token_grads, "pipe", -1)
    hot_up_part, hot_down_part = group_reduce_scatter(
        (rep_up_sum.astype(jnp.bfloat16), rep_down_sum.astype(jnp.bfloat16)), local_pos
    )
    hot_up_part = hot_up_part.astype(jnp.bfloat16)
    hot_down_part = hot_down_part.astype(jnp.bfloat16)
    up_grad = own_up_sum.astype(jnp.bfloat16)
    down_grad = own_down_sum.astype(jnp.bfloat16)
    gate_grads = jnp.stack([member[1] for member in outputs], 0)
    return (
        sent_back[None],
        up_grad[None, None],
        down_grad[None, None],
        gate_grads[None, :, None],
        hot_up_part[None, None],
        hot_down_part[None, None],
    )


EXPERT = ("grp", "j")


def solution(mesh):
    groups = mesh.devices.reshape(mesh.shape["pipe"], -1, REPL)
    group_mesh = jax.sharding.Mesh(groups, ("pipe", "grp", "j"))
    return jax.shard_map(
        per_device,
        mesh=group_mesh,
        in_specs=(
            P("pipe", None, EXPERT, None),
            P("pipe", None, EXPERT, None),
            P("pipe", None, EXPERT, None),
            P("pipe", None),
            P("pipe", EXPERT, None, None),
            P("pipe", EXPERT, None, None),
            P("pipe", None, EXPERT, None, None, None),
            P("pipe", None, EXPERT, None, None, None),
        ),
        out_specs=(
            P("pipe", None, EXPERT, None),
            P("pipe", EXPERT, None, None),
            P("pipe", EXPERT, None, None),
            P("pipe", None, EXPERT, None, None, None),
            P("pipe", EXPERT, None, None),
            P("pipe", EXPERT, None, None),
        ),
        check_vma=False,
    )
```
